256 devices in a mesh: replica: 8 (over y, core), fsdp: 32 (over x, z).
Axes of the slice: x: 4, y: 4, z: 8, core: 2. Of those that a mesh axis runs over, the one named last changes fastest.
Arguments:
- anchor_params: bfloat16 [24, 512, 4096], P(None, 'fsdp')
- replica_params: bfloat16 [8, 24, 512, 4096], P('replica', None, 'fsdp')
- projection: bfloat16 [4096, 384], replicated
- momentum: float32 [24, 512, 384], P(None, 'fsdp'), may hold values from -1.8 to 1.8
- rate_table: float32 [4, 6], replicated, may hold values from 0.1 to 1
- owner_list: int32 [24], replicated, may hold values from 0 to 31, as said below
- layer_kind: int32 [24, 2], replicated, may hold values from 0 to 5, as said below
Outputs:
- new_params: bfloat16 [24, 512, 4096], P(None, 'fsdp')
- new_momentum: float32 [24, 512, 384], P(None, 'fsdp')
The draws below stay inside these ranges and needn't reach their ends.
Inputs may be any that keep to these rules, and one draw needn't show every extreme that they name: `owner_list`: no fsdp index is named more than 2 times, and in every draw some index is named exactly 2 times. `layer_kind`: column 0 is a layer, column 1 a kind below 6; each layer has 6 rows, and no two rows are equal.
All inputs are finite; a program needn't handle non-finite values.
Results may differ from the reference program's by a relative error of at most 0.0055.
Values may be sent and summed in bfloat16 or wider, within the bound.
No kernel may reach another device: no remote copies, remote signals or barrier semaphores. Data moves between devices by JAX's collectives and lax.ppermute only.
A program may use at most 128 MiB of HBM per device.

```python
import math
import jax
import jax.numpy as jnp
from jax import lax

D = 4096
R = 384
ROWS = 512
MATS = 24
LAYERS = 4
KINDS = 6
OWN_MOST = 2
N_REPLICA = 8
N_FSDP = 32


def anchor_values(key):
    anchor_key = jax.random.fold_in(key, 1)
    values = jax.random.normal(anchor_key, (MATS, ROWS, D), jnp.float32)
    return values


def draw_anchor_params(key, part):
    return anchor_values(key).astype(jnp.bfloat16)


def draw_replica_params(key, part):
    anchor = anchor_values(key)
    row_key = jax.random.fold_in(key, 2)
    matrix_key = jax.random.fold_in(key, 3)
    noise_key = jax.random.fold_in(key, 4)
    row_scale = jnp.exp(jax.random.uniform(row_key, (MATS, ROWS), jnp.float32, 0.0, math.log(10.0)))
    ramp = 1.0 + 2.0 * jnp.arange(ROWS, dtype=jnp.float32) / max(ROWS - 1, 1)
    matrix_scale = jnp.exp(jax.random.uniform(matrix_key, (MATS,), jnp.float32, math.log(0.3), math.log(3.0)))
    spread = 0.02 * row_scale * ramp[None, :] * matrix_scale[:, None]
    noise = jax.random.normal(noise_key, (N_REPLICA, MATS, ROWS, D), jnp.float32)
    return (anchor[None] + noise * spread[None, :, :, None]).astype(jnp.bfloat16)


def draw_projection(key, part):
    value_key = jax.random.fold_in(key, 6)
    column_key = jax.random.fold_in(key, 7)
    column_scale = jnp.exp(jax.random.uniform(column_key, (R,), jnp.float32, 0.0, math.log(10.0)))
    values = jax.random.normal(value_key, (D, R), jnp.float32)
    return (values * column_scale[None, :] / math.sqrt(D)).astype(jnp.bfloat16)


def draw_owner_list(key, part):
    first_key = jax.random.fold_in(key, 20)
    rest_key = jax.random.fold_in(key, 21)
    order_key = jax.random.fold_in(key, 22)
    first = jax.random.randint(first_key, (), 0, N_FSDP)
    others = jax.random.permutation(rest_key, OWN_MOST * (N_FSDP - 1))[:MATS - OWN_MOST]
    rest = (first + 1 + others % (N_FSDP - 1)) % N_FSDP
    listed = jnp.concatenate([jnp.full((OWN_MOST,), first, jnp.int32), rest.astype(jnp.int32)])
    shifted = (listed + (N_FSDP - 1 - jnp.max(listed))) % N_FSDP
    order = jax.random.permutation(order_key, MATS)
    return shifted[order].astype(jnp.int32)


def draw_layer_kind(key, part):
    per_layer = MATS // LAYERS
    kind_parts = []
    for layer_index in range(LAYERS):
        layer_key = jax.random.fold_in(key, 40 + layer_index)
        if layer_index == 0:
            chosen = jnp.concatenate([jnp.full((1,), KINDS - 1, jnp.int32), jax.random.permutation(layer_key, KINDS - 1)[:per_layer - 1].astype(jnp.int32)])
        else:
            chosen = jax.random.permutation(layer_key, KINDS)[:per_layer].astype(jnp.int32)
        kind_parts.append(chosen)
    kinds = jnp.concatenate(kind_parts)
    layers = jnp.arange(MATS, dtype=jnp.int32) // per_layer
    table = jnp.stack([layers, kinds], axis=1)
    order = jax.random.permutation(jax.random.fold_in(key, 60), MATS)
    return table[order].astype(jnp.int32)


def block_levels(rng, shape, cuts, smallest, top_value):
    gain, own = 1.0, jax.random.fold_in(rng, 6)
    for dim, shards_of in cuts:
        draws = jnp.exp(jax.random.uniform(jax.random.fold_in(own, dim), (shards_of,), jnp.float32, smallest / len(cuts), top_value / len(cuts)))
        gain = gain * jnp.repeat(draws, shape[dim] // shards_of).reshape([-1 if axis == dim else 1 for axis in range(len(shape))])
    return gain


def scatter_about(key, extent, scale, most, pieces=(), kind=jnp.bfloat16):
    array = scale * jax.random.normal(key, extent, jnp.float32)
    if pieces:
        array = array * block_levels(key, extent, pieces, -0.22, 0.18)
    return jnp.clip(array, -most, most).astype(kind)


def setup_inputs(seed: int = 0) -> dict:
    arg_keys = jax.random.split(jax.random.key(seed), 8)
    return {
        "anchor_params": draw_anchor_params(jax.random.fold_in(arg_keys[7], 71), 0),
        "replica_params": draw_replica_params(jax.random.fold_in(arg_keys[7], 71), 0),
        "projection": draw_projection(jax.random.fold_in(arg_keys[7], 71), 0),
        "momentum": scatter_about(arg_keys[3], (MATS, ROWS, R), 0.3, 1.8, ((1, 32),), jnp.float32),
        "rate_table": jnp.clip(jnp.exp(jax.random.uniform(arg_keys[4], (LAYERS, KINDS), jnp.float32, math.log(0.1), math.log(1.0))), 0.1, 1.0),
        "owner_list": draw_owner_list(jax.random.fold_in(arg_keys[7], 71), 0),
        "layer_kind": draw_layer_kind(jax.random.fold_in(arg_keys[7], 71), 0),
    }


OUTER_MOMENTUM = 0.9
EPSILON = 1e-06

def reference(anchor_params, replica_params, projection, momentum, rate_table, owner_list, layer_kind):
    summed = jnp.zeros((MATS, ROWS, R), jnp.float32)
    for replica_index in range(N_REPLICA):
        pseudo_grad = (anchor_params.astype(jnp.float32) - replica_params[replica_index].astype(jnp.float32)).astype(jnp.bfloat16)
        compressed = jnp.dot(pseudo_grad.reshape(MATS * ROWS, D), projection, preferred_element_type=jnp.float32)
        summed = summed + compressed.reshape(MATS, ROWS, R)
    outer_grad = summed / N_REPLICA
    new_momentum = OUTER_MOMENTUM * momentum + outer_grad
    outer_step = outer_grad + OUTER_MOMENTUM * new_momentum
    squares = lax.optimization_barrier(jnp.sum(outer_step * outer_step, axis=(1, 2)))
    same_group = (owner_list[:, None] == owner_list[None, :]).astype(jnp.float32)
    group_squares = jnp.dot(same_group, squares, precision=lax.Precision.HIGHEST)
    group_count = lax.optimization_barrier(jnp.sum(same_group, axis=1))
    scaling = lax.rsqrt(group_squares / (group_count * (ROWS * R)) + EPSILON)
    outer_rate = rate_table[layer_kind[:, 0], layer_kind[:, 1]]
    direction = (outer_step * (outer_rate * scaling)[:, None, None]).astype(jnp.bfloat16)
    update = lax.dot_general(direction.reshape(MATS * ROWS, R), projection, (((1,), (1,)), ((), ())), preferred_element_type=jnp.float32).astype(jnp.bfloat16)
    new_params = (anchor_params.astype(jnp.float32) - update.reshape(MATS, ROWS, D).astype(jnp.float32)).astype(jnp.bfloat16)
    return (new_params, new_momentum)
```

```python
import jax
import jax.numpy as jnp
from jax import lax
from jax.sharding import PartitionSpec as P

OUTER_MOMENTUM = 0.9
EPSILON = 1e-06


def local(anchor_params, replica_params, projection, momentum, rate_table, owner_list, layer_kind):
    matrices, rows_dev, model_width = anchor_params.shape
    rank_dim = projection.shape[1]
    all_rows = rows_dev * lax.axis_size("fsdp")
    highest = lax.Precision.HIGHEST
    pseudo_grad = (
        anchor_params.astype(jnp.float32) - replica_params[0].astype(jnp.float32)
    ).astype(jnp.bfloat16)
    compressed = jnp.dot(
        pseudo_grad.reshape(matrices * rows_dev, model_width),
        projection,
        preferred_element_type=jnp.float32,
    )
    summed = lax.psum(compressed.reshape(matrices, rows_dev, rank_dim), "replica")
    outer_grad = summed / lax.axis_size("replica")
    new_momentum = OUTER_MOMENTUM * momentum + outer_grad
    outer_step = outer_grad + OUTER_MOMENTUM * new_momentum
    squares = lax.psum(jnp.sum(outer_step * outer_step, axis=(1, 2)), "fsdp")
    same_group = (owner_list[:, None] == owner_list[None, :]).astype(jnp.float32)
    group_squares = jnp.dot(same_group, squares, precision=highest)
    group_count = jnp.sum(same_group, axis=1)
    scaling = lax.rsqrt(group_squares / (group_count * (all_rows * rank_dim)) + EPSILON)
    outer_rate = rate_table[layer_kind[:, 0], layer_kind[:, 1]]
    direction = (outer_step * (outer_rate * scaling)[:, None, None]).astype(jnp.bfloat16)
    update = lax.dot_general(
        direction.reshape(matrices * rows_dev, rank_dim),
        projection,
        (((1,), (1,)), ((), ())),
        preferred_element_type=jnp.float32,
    ).astype(jnp.bfloat16)
    new_params = (
        anchor_params.astype(jnp.float32)
        - update.reshape(matrices, rows_dev, model_width).astype(jnp.float32)
    ).astype(jnp.bfloat16)
    return (new_params, new_momentum)


def solution(mesh):
    placed = (
        P(None, "fsdp", None),
        P("replica", None, "fsdp", None),
        P(),
        P(None, "fsdp", None),
        P(),
        P(),
        P(),
    )
    return jax.shard_map(
        local,
        mesh=mesh,
        in_specs=placed,
        out_specs=(P(None, "fsdp", None), P(None, "fsdp", None)),
        check_vma=False,
    )
```

```python
import jax
import jax.numpy as jnp
from jax import lax
from jax.sharding import PartitionSpec as P

OUTER_MOMENTUM = 0.9
EPSILON = 1e-06

def butterfly(x, axis):
    size = lax.axis_size(axis)
    step = 1
    while step < size:
        perm = [(i, i ^ step) for i in range(size)]
        x = x + lax.ppermute(x, axis, perm)
        step *= 2
    return x


def local(anchor_params, replica_params, projection, momentum, rate_table, owner_list, layer_kind):
    matrices, rows_dev, model_width = anchor_params.shape
    rank_dim = projection.shape[1]
    all_rows = rows_dev * lax.axis_size("fsdp")
    highest = lax.Precision.HIGHEST
    pseudo_grad = (
        anchor_params.astype(jnp.float32) - replica_params[0].astype(jnp.float32)
    ).astype(jnp.bfloat16)
    compressed = jnp.dot(
        pseudo_grad.reshape(matrices * rows_dev, model_width),
        projection,
        preferred_element_type=jnp.float32,
    )
    summed = butterfly(compressed.reshape(matrices, rows_dev, rank_dim), "replica")
    outer_grad = summed / lax.axis_size("replica")
    new_momentum = OUTER_MOMENTUM * momentum + outer_grad
    outer_step = outer_grad + OUTER_MOMENTUM * new_momentum
    squares = butterfly(jnp.sum(outer_step * outer_step, axis=(1, 2)), "fsdp")
    same_group = (owner_list[:, None] == owner_list[None, :]).astype(jnp.float32)
    group_squares = jnp.dot(same_group, squares, precision=highest)
    group_count = jnp.sum(same_group, axis=1)
    scaling = lax.rsqrt(group_squares / (group_count * (all_rows * rank_dim)) + EPSILON)
    outer_rate = rate_table[layer_kind[:, 0], layer_kind[:, 1]]
    direction = (outer_step * (outer_rate * scaling)[:, None, None]).astype(jnp.bfloat16)
    update = lax.dot_general(
        direction.reshape(matrices * rows_dev, rank_dim),
        projection,
        (((1,), (1,)), ((), ())),
        preferred_element_type=jnp.float32,
    ).astype(jnp.bfloat16)
    new_params = (
        anchor_params.astype(jnp.float32)
        - update.reshape(matrices, rows_dev, model_width).astype(jnp.float32)
    ).astype(jnp.bfloat16)
    return (new_params, new_momentum)


def solution(mesh):
    placed = (
        P(None, "fsdp", None),
        P("replica", None, "fsdp", None),
        P(),
        P(None, "fsdp", None),
        P(),
        P(),
        P(),
    )
    return jax.shard_map(
        local,
        mesh=mesh,
        in_specs=placed,
        out_specs=(P(None, "fsdp", None), P(None, "fsdp", None)),
        check_vma=False,
    )
```

```python
import jax
import jax.numpy as jnp
from jax import lax
from jax.sharding import PartitionSpec as P

OUTER_MOMENTUM = 0.9
EPSILON = 1e-06

def butterfly(x, axis):
    size = lax.axis_size(axis)
    step = 1
    while step < size:
        perm = [(i, i ^ step) for i in range(size)]
        x = x + lax.ppermute(x, axis, perm)
        step *= 2
    return x


def replica_sum(x, axis):
    size = lax.axis_size(axis)
    chips = size // 2
    if size % 2 or chips != 4:
        return butterfly(x, axis)
    core = lax.axis_index(axis) % 2
    swap = [(i, i ^ 1) for i in range(size)]
    half = x.shape[0] // 2
    keep = lax.dynamic_slice_in_dim(x, core * half, half)
    send = lax.dynamic_slice_in_dim(x, (1 - core) * half, half)
    x = keep + lax.ppermute(send, axis, swap)
    even = [(0, 1), (2, 3)]
    odd = [(1, 2), (3, 0)]
    for step in range(2):
        perm = []
        for c in range(2):
            for a, b in (even if c == step else odd):
                perm += [(a * 2 + c, b * 2 + c), (b * 2 + c, a * 2 + c)]
        x = x + lax.ppermute(x, axis, perm)
    other = lax.ppermute(x, axis, swap)
    return jnp.where(core == 1, jnp.concatenate([other, x]), jnp.concatenate([x, other]))


def local(anchor_params, replica_params, projection, momentum, rate_table, owner_list, layer_kind):
    matrices, rows_dev, model_width = anchor_params.shape
    rank_dim = projection.shape[1]
    all_rows = rows_dev * lax.axis_size("fsdp")
    highest = lax.Precision.HIGHEST
    pseudo_grad = (
        anchor_params.astype(jnp.float32) - replica_params[0].astype(jnp.float32)
    ).astype(jnp.bfloat16)
    compressed = jnp.dot(
        pseudo_grad.reshape(matrices * rows_dev, model_width),
        projection,
        preferred_element_type=jnp.float32,
    )
    summed = replica_sum(compressed.reshape(matrices, rows_dev, rank_dim), "replica")
    outer_grad = summed / lax.axis_size("replica")
    new_momentum = OUTER_MOMENTUM * momentum + outer_grad
    outer_step = outer_grad + OUTER_MOMENTUM * new_momentum
    squares = jnp.sum(lax.all_to_all(jnp.broadcast_to(jnp.sum(outer_step * outer_step, axis=(1, 2)), (lax.axis_size("fsdp"), outer_step.shape[0])), "fsdp", 0, 0, tiled=True), axis=0)
    same_group = (owner_list[:, None] == owner_list[None, :]).astype(jnp.float32)
    group_squares = jnp.dot(same_group, squares, precision=highest)
    group_count = jnp.sum(same_group, axis=1)
    scaling = lax.rsqrt(group_squares / (group_count * (all_rows * rank_dim)) + EPSILON)
    outer_rate = rate_table[layer_kind[:, 0], layer_kind[:, 1]]
    direction = (outer_step * (outer_rate * scaling)[:, None, None]).astype(jnp.bfloat16)
    update = lax.dot_general(
        direction.reshape(matrices * rows_dev, rank_dim),
        projection,
        (((1,), (1,)), ((), ())),
        preferred_element_type=jnp.float32,
    ).astype(jnp.bfloat16)
    new_params = (
        anchor_params.astype(jnp.float32)
        - update.reshape(matrices, rows_dev, model_width).astype(jnp.float32)
    ).astype(jnp.bfloat16)
    return (new_params, new_momentum)


def solution(mesh):
    placed = (
        P(None, "fsdp", None),
        P("replica", None, "fsdp", None),
        P(),
        P(None, "fsdp", None),
        P(),
        P(),
        P(),
    )
    return jax.shard_map(
        local,
        mesh=mesh,
        in_specs=placed,
        out_specs=(P(None, "fsdp", None), P(None, "fsdp", None)),
        check_vma=False,
    )
```

```python
import jax
import jax.numpy as jnp
from jax import lax
from jax.sharding import PartitionSpec as P

OUTER_MOMENTUM = 0.9
EPSILON = 1e-06

def ring_steps(x, axis):
    even = [(0, 1), (2, 3)]
    odd = [(1, 2), (3, 0)]
    for step in range(2):
        perm = []
        for c in range(2):
            for a, b in (even if c == step else odd):
                perm += [(a * 2 + c, b * 2 + c), (b * 2 + c, a * 2 + c)]
        x = x + lax.ppermute(x, axis, perm)
    return x


def a2a_sum(v, axis):
    n = lax.axis_size(axis)
    return jnp.sum(lax.all_to_all(jnp.broadcast_to(v, (n,) + v.shape), axis, 0, 0, tiled=True), axis=0)


def local(anchor_params, replica_params, projection, momentum, rate_table, owner_list, layer_kind):
    matrices, rows_dev, model_width = anchor_params.shape
    rank_dim = projection.shape[1]
    all_rows = rows_dev * lax.axis_size("fsdp")
    n_replica = lax.axis_size("replica")
    highest = lax.Precision.HIGHEST
    half = matrices // 2
    core = lax.axis_index("replica") % 2
    swap = [(i, i ^ 1) for i in range(n_replica)]

    def compress(first):
        anchor = lax.dynamic_slice_in_dim(anchor_params, first, half)
        replica = lax.dynamic_slice_in_dim(replica_params[0], first, half)
        pseudo_grad = (anchor.astype(jnp.float32) - replica.astype(jnp.float32)).astype(jnp.bfloat16)
        return jnp.dot(
            pseudo_grad.reshape(half * rows_dev, model_width), projection, preferred_element_type=jnp.float32
        ).reshape(half, rows_dev, rank_dim)

    outgoing = lax.ppermute(compress((1 - core) * half), "replica", swap)
    own = ring_steps(compress(core * half) + outgoing, "replica")
    own_grad = own / n_replica
    own_momentum = OUTER_MOMENTUM * lax.dynamic_slice_in_dim(momentum, core * half, half) + own_grad
    own_step = own_grad + OUTER_MOMENTUM * own_momentum
    own_squares = a2a_sum(jnp.sum(own_step * own_step, axis=(1, 2)), "fsdp")
    other = lax.ppermute(own, "replica", swap)
    summed = jnp.where(core == 1, jnp.concatenate([other, own]), jnp.concatenate([own, other]))
    outer_grad = summed / n_replica
    new_momentum = OUTER_MOMENTUM * momentum + outer_grad
    outer_step = outer_grad + OUTER_MOMENTUM * new_momentum
    other_squares = lax.ppermute(own_squares, "replica", swap)
    squares = jnp.where(
        core == 1,
        jnp.concatenate([other_squares, own_squares]),
        jnp.concatenate([own_squares, other_squares]),
    )
    same_group = (owner_list[:, None] == owner_list[None, :]).astype(jnp.float32)
    group_squares = jnp.dot(same_group, squares, precision=highest)
    group_count = jnp.sum(same_group, axis=1)
    scaling = lax.rsqrt(group_squares / (group_count * (all_rows * rank_dim)) + EPSILON)
    outer_rate = rate_table[layer_kind[:, 0], layer_kind[:, 1]]
    direction = (outer_step * (outer_rate * scaling)[:, None, None]).astype(jnp.bfloat16)
    update = lax.dot_general(
        direction.reshape(matrices * rows_dev, rank_dim),
        projection,
        (((1,), (1,)), ((), ())),
        preferred_element_type=jnp.float32,
    ).astype(jnp.bfloat16)
    new_params = (
        anchor_params.astype(jnp.float32)
        - update.reshape(matrices, rows_dev, model_width).astype(jnp.float32)
    ).astype(jnp.bfloat16)
    return (new_params, new_momentum)


def solution(mesh):
    placed = (
        P(None, "fsdp", None),
        P("replica", None, "fsdp", None),
        P(),
        P(None, "fsdp", None),
        P(),
        P(),
        P(),
    )
    return jax.shard_map(
        local,
        mesh=mesh,
        in_specs=placed,
        out_specs=(P(None, "fsdp", None), P(None, "fsdp", None)),
        check_vma=False,
    )
```

```python
import jax
import jax.numpy as jnp
from jax import lax
from jax.sharding import PartitionSpec as P

OUTER_MOMENTUM = 0.9
EPSILON = 1e-06

def ring_steps(x, axis):
    even = [(0, 1), (2, 3)]
    odd = [(1, 2), (3, 0)]
    for step in range(2):
        perm = []
        for c in range(2):
            for a, b in (even if c == step else odd):
                perm += [(a * 2 + c, b * 2 + c), (b * 2 + c, a * 2 + c)]
        x = x + lax.ppermute(x, axis, perm)
    return x


def a2a_sum(v, axis):
    n = lax.axis_size(axis)
    return jnp.sum(lax.all_to_all(jnp.broadcast_to(v, (n,) + v.shape), axis, 0, 0, tiled=True), axis=0)


def local(anchor_params, replica_params, projection, momentum, rate_table, owner_list, layer_kind):
    matrices, rows_dev, model_width = anchor_params.shape
    rank_dim = projection.shape[1]
    all_rows = rows_dev * lax.axis_size("fsdp")
    n_replica = lax.axis_size("replica")
    highest = lax.Precision.HIGHEST
    half = matrices // 2
    core = lax.axis_index("replica") % 2
    swap = [(i, i ^ 1) for i in range(n_replica)]

    def compress(first):
        anchor = lax.dynamic_slice_in_dim(anchor_params, first, half)
        replica = lax.dynamic_slice_in_dim(replica_params[0], first, half)
        pseudo_grad = (anchor.astype(jnp.float32) - replica.astype(jnp.float32)).astype(jnp.bfloat16)
        return jnp.dot(
            pseudo_grad.reshape(half * rows_dev, model_width), projection, preferred_element_type=jnp.float32
        ).reshape(half, rows_dev, rank_dim)

    outgoing = lax.ppermute(compress((1 - core) * half), "replica", swap)
    own = ring_steps(lax.optimization_barrier(compress(core * half)) + outgoing, "replica")
    own_grad = own / n_replica
    own_momentum = OUTER_MOMENTUM * lax.dynamic_slice_in_dim(momentum, core * half, half) + own_grad
    own_step = own_grad + OUTER_MOMENTUM * own_momentum
    own_squares = a2a_sum(jnp.sum(own_step * own_step, axis=(1, 2)), "fsdp")
    other = lax.ppermute(own, "replica", swap)
    summed = jnp.where(core == 1, jnp.concatenate([other, own]), jnp.concatenate([own, other]))
    outer_grad = summed / n_replica
    new_momentum = OUTER_MOMENTUM * momentum + outer_grad
    outer_step = outer_grad + OUTER_MOMENTUM * new_momentum
    other_squares = lax.ppermute(own_squares, "replica", swap)
    squares = jnp.where(
        core == 1,
        jnp.concatenate([other_squares, own_squares]),
        jnp.concatenate([own_squares, other_squares]),
    )
    same_group = (owner_list[:, None] == owner_list[None, :]).astype(jnp.float32)
    group_squares = jnp.dot(same_group, squares, precision=highest)
    group_count = jnp.sum(same_group, axis=1)
    scaling = lax.rsqrt(group_squares / (group_count * (all_rows * rank_dim)) + EPSILON)
    outer_rate = rate_table[layer_kind[:, 0], layer_kind[:, 1]]
    direction = (outer_step * (outer_rate * scaling)[:, None, None]).astype(jnp.bfloat16)
    update = lax.dot_general(
        direction.reshape(matrices * rows_dev, rank_dim),
        projection,
        (((1,), (1,)), ((), ())),
        preferred_element_type=jnp.float32,
    ).astype(jnp.bfloat16)
    new_params = (
        anchor_params.astype(jnp.float32)
        - update.reshape(matrices, rows_dev, model_width).astype(jnp.float32)
    ).astype(jnp.bfloat16)
    return (new_params, new_momentum)


def solution(mesh):
    placed = (
        P(None, "fsdp", None),
        P("replica", None, "fsdp", None),
        P(),
        P(None, "fsdp", None),
        P(),
        P(),
        P(),
    )
    return jax.shard_map(
        local,
        mesh=mesh,
        in_specs=placed,
        out_specs=(P(None, "fsdp", None), P(None, "fsdp", None)),
        check_vma=False,
    )
```

```python
import jax
import jax.numpy as jnp
from jax import lax
from jax.experimental import pallas as pl
from jax.sharding import PartitionSpec as P


OUTER_MOMENTUM = 0.9
EPSILON = 1e-06


def apply_update(direction, projection_t, anchor, block=2048):
    rows, rank_dim = direction.shape
    model_width = projection_t.shape[1]

    def body(direction_ref, proj_ref, anchor_ref, out_ref):
        update = jnp.dot(direction_ref[...], proj_ref[...], preferred_element_type=jnp.float32)
        update = update.astype(jnp.bfloat16).astype(jnp.float32)
        out_ref[...] = (anchor_ref[...].astype(jnp.float32) - update).astype(jnp.bfloat16)

    return pl.pallas_call(
        body,
        grid=(model_width // block,),
        in_specs=[
            pl.BlockSpec((rows, rank_dim), lambda j: (0, 0)),
            pl.BlockSpec((rank_dim, block), lambda j: (0, j)),
            pl.BlockSpec((rows, block), lambda j: (0, j)),
        ],
        out_specs=pl.BlockSpec((rows, block), lambda j: (0, j)),
        out_shape=jax.ShapeDtypeStruct((rows, model_width), jnp.bfloat16),
    )(direction, projection_t, anchor)


def ring_steps(x, axis):
    even = [(0, 1), (2, 3)]
    odd = [(1, 2), (3, 0)]
    for step in range(2):
        perm = []
        for c in range(2):
            for a, b in (even if c == step else odd):
                perm += [(a * 2 + c, b * 2 + c), (b * 2 + c, a * 2 + c)]
        x = x + lax.ppermute(x, axis, perm)
    return x


def a2a_sum(v, axis):
    n = lax.axis_size(axis)
    return jnp.sum(lax.all_to_all(jnp.broadcast_to(v, (n,) + v.shape), axis, 0, 0, tiled=True), axis=0)


def local(anchor_params, replica_params, projection, momentum, rate_table, owner_list, layer_kind):
    matrices, rows_dev, model_width = anchor_params.shape
    rank_dim = projection.shape[1]
    all_rows = rows_dev * lax.axis_size("fsdp")
    n_replica = lax.axis_size("replica")
    highest = lax.Precision.HIGHEST
    half = matrices // 2
    core = lax.axis_index("replica") % 2
    swap = [(i, i ^ 1) for i in range(n_replica)]

    def compress(first):
        anchor = lax.dynamic_slice_in_dim(anchor_params, first, half)
        replica = lax.dynamic_slice_in_dim(replica_params[0], first, half)
        pseudo_grad = (anchor.astype(jnp.float32) - replica.astype(jnp.float32)).astype(jnp.bfloat16)
        return jnp.dot(
            pseudo_grad.reshape(half * rows_dev, model_width), projection, preferred_element_type=jnp.float32
        ).reshape(half, rows_dev, rank_dim)

    outgoing = lax.ppermute(compress((1 - core) * half), "replica", swap)
    own = ring_steps(lax.optimization_barrier(compress(core * half)) + outgoing, "replica")
    own_grad = own / n_replica
    own_momentum = OUTER_MOMENTUM * lax.dynamic_slice_in_dim(momentum, core * half, half) + own_grad
    own_step = own_grad + OUTER_MOMENTUM * own_momentum
    own_squares = a2a_sum(jnp.sum(own_step * own_step, axis=(1, 2)), "fsdp")
    other = lax.ppermute(own, "replica", swap)
    summed = jnp.where(core == 1, jnp.concatenate([other, own]), jnp.concatenate([own, other]))
    outer_grad = summed / n_replica
    new_momentum = OUTER_MOMENTUM * momentum + outer_grad
    outer_step = outer_grad + OUTER_MOMENTUM * new_momentum
    new_momentum, outer_step = lax.optimization_barrier((new_momentum, outer_step))
    other_squares = lax.ppermute(own_squares, "replica", swap)
    squares = jnp.where(
        core == 1,
        jnp.concatenate([other_squares, own_squares]),
        jnp.concatenate([own_squares, other_squares]),
    )
    same_group = (owner_list[:, None] == owner_list[None, :]).astype(jnp.float32)
    group_count = jnp.sum(same_group, axis=1)
    outer_rate = rate_table[layer_kind[:, 0], layer_kind[:, 1]]
    projection_t = projection.T
    group_squares = jnp.dot(same_group, squares, precision=highest)
    scaling = lax.rsqrt(group_squares / (group_count * (all_rows * rank_dim)) + EPSILON)
    direction = (outer_step * (outer_rate * scaling)[:, None, None]).astype(jnp.bfloat16)
    new_params = apply_update(
        direction.reshape(matrices * rows_dev, rank_dim),
        projection_t,
        anchor_params.reshape(matrices * rows_dev, model_width),
    ).reshape(matrices, rows_dev, model_width)
    return (new_params, new_momentum)


def solution(mesh):
    placed = (
        P(None, "fsdp", None),
        P("replica", None, "fsdp", None),
        P(),
        P(None, "fsdp", None),
        P(),
        P(),
        P(),
    )
    return jax.shard_map(
        local,
        mesh=mesh,
        in_specs=placed,
        out_specs=(P(None, "fsdp", None), P(None, "fsdp", None)),
        check_vma=False,
    )
```

```python
import jax
import jax.numpy as jnp
from jax import lax
from jax.experimental import pallas as pl
from jax.experimental.pallas import tpu as pltpu
from jax.sharding import PartitionSpec as P


OUTER_MOMENTUM = 0.9
EPSILON = 1e-06


def apply_update(outer_step, coef, projection_t, anchor, block=2048):
    rows, rank_dim = outer_step.shape
    model_width = projection_t.shape[1]
    per = rows // coef.shape[0]

    def body(step_ref, coef_ref, proj_ref, anchor_ref, out_ref, direction_ref):
        @pl.when(pl.program_id(0) == 0)
        def _():
            for m in range(coef.shape[0]):
                part = step_ref[m * per:(m + 1) * per, :] * coef_ref[m]
                direction_ref[m * per:(m + 1) * per, :] = part.astype(jnp.bfloat16)

        update = jnp.dot(direction_ref[...], proj_ref[...], preferred_element_type=jnp.float32)
        update = update.astype(jnp.bfloat16).astype(jnp.float32)
        out_ref[...] = (anchor_ref[...].astype(jnp.float32) - update).astype(jnp.bfloat16)

    return pl.pallas_call(
        body,
        grid=(model_width // block,),
        in_specs=[
            pl.BlockSpec((rows, rank_dim), lambda j: (0, 0)),
            pl.BlockSpec(memory_space=pltpu.SMEM),
            pl.BlockSpec((rank_dim, block), lambda j: (0, j)),
            pl.BlockSpec((rows, block), lambda j: (0, j)),
        ],
        out_specs=pl.BlockSpec((rows, block), lambda j: (0, j)),
        out_shape=jax.ShapeDtypeStruct((rows, model_width), jnp.bfloat16),
        scratch_shapes=[pltpu.VMEM((rows, rank_dim), jnp.bfloat16)],
    )(outer_step, coef, projection_t, anchor)


def ring_steps(x, axis):
    even = [(0, 1), (2, 3)]
    odd = [(1, 2), (3, 0)]
    for step in range(2):
        perm = []
        for c in range(2):
            for a, b in (even if c == step else odd):
                perm += [(a * 2 + c, b * 2 + c), (b * 2 + c, a * 2 + c)]
        x = x + lax.ppermute(x, axis, perm)
    return x


def a2a_sum(v, axis):
    n = lax.axis_size(axis)
    return jnp.sum(lax.all_to_all(jnp.broadcast_to(v, (n,) + v.shape), axis, 0, 0, tiled=True), axis=0)


def local(anchor_params, replica_params, projection, momentum, rate_table, owner_list, layer_kind):
    matrices, rows_dev, model_width = anchor_params.shape
    rank_dim = projection.shape[1]
    all_rows = rows_dev * lax.axis_size("fsdp")
    n_replica = lax.axis_size("replica")
    highest = lax.Precision.HIGHEST
    half = matrices // 2
    core = lax.axis_index("replica") % 2
    swap = [(i, i ^ 1) for i in range(n_replica)]

    def compress(first):
        anchor = lax.dynamic_slice_in_dim(anchor_params, first, half)
        replica = lax.dynamic_slice_in_dim(replica_params[0], first, half)
        pseudo_grad = (anchor.astype(jnp.float32) - replica.astype(jnp.float32)).astype(jnp.bfloat16)
        return jnp.dot(
            pseudo_grad.reshape(half * rows_dev, model_width), projection, preferred_element_type=jnp.float32
        ).reshape(half, rows_dev, rank_dim)

    outgoing = lax.ppermute(compress((1 - core) * half), "replica", swap)
    own = ring_steps(lax.optimization_barrier(compress(core * half)) + outgoing, "replica")
    own_grad = own / n_replica
    own_momentum = OUTER_MOMENTUM * lax.dynamic_slice_in_dim(momentum, core * half, half) + own_grad
    own_step = own_grad + OUTER_MOMENTUM * own_momentum
    own_squares = a2a_sum(jnp.sum(own_step * own_step, axis=(1, 2)), "fsdp")
    other = lax.ppermute(own, "replica", swap)
    summed = jnp.where(core == 1, jnp.concatenate([other, own]), jnp.concatenate([own, other]))
    outer_grad = summed / n_replica
    new_momentum = OUTER_MOMENTUM * momentum + outer_grad
    outer_step = outer_grad + OUTER_MOMENTUM * new_momentum
    new_momentum, outer_step = lax.optimization_barrier((new_momentum, outer_step))
    other_squares = lax.ppermute(own_squares, "replica", swap)
    squares = jnp.where(
        core == 1,
        jnp.concatenate([other_squares, own_squares]),
        jnp.concatenate([own_squares, other_squares]),
    )
    same_group = (owner_list[:, None] == owner_list[None, :]).astype(jnp.float32)
    group_count = jnp.sum(same_group, axis=1)
    outer_rate = rate_table[layer_kind[:, 0], layer_kind[:, 1]]
    projection_t = projection.T
    group_squares = jnp.dot(same_group, squares, precision=highest)
    scaling = lax.rsqrt(group_squares / (group_count * (all_rows * rank_dim)) + EPSILON)
    new_params = apply_update(
        outer_step.reshape(matrices * rows_dev, rank_dim),
        outer_rate * scaling,
        projection_t,
        anchor_params.reshape(matrices * rows_dev, model_width),
    ).reshape(matrices, rows_dev, model_width)
    return (new_params, new_momentum)


def solution(mesh):
    placed = (
        P(None, "fsdp", None),
        P("replica", None, "fsdp", None),
        P(),
        P(None, "fsdp", None),
        P(),
        P(),
        P(),
    )
    return jax.shard_map(
        local,
        mesh=mesh,
        in_specs=placed,
        out_specs=(P(None, "fsdp", None), P(None, "fsdp", None)),
        check_vma=False,
    )
```
